256 devices in a mesh: gx: 8 (over x, core), gy: 16 (over y, z_lo), lev: 2 (over z_hi).
Axes of the slice: x: 4, y: 4, z: 8 (z_hi: 2, z_lo: 4; z = z_hi * 4 + z_lo), core: 2. Of those that a mesh axis runs over, the one named last changes fastest.
Arguments:
- source: float32 [32, 512, 1024], P('lev', 'gy', 'gx'), may hold values from -6 to 6
- remap_weights: float32 [4096, 4, 128, 128], P(('gx', 'gy'))
- intersection_devices: int32 [4096, 4], replicated, may hold values from 0 to 127, all different within a row; in each aligned block of 32 rows (0 to 31, 32 to 63, ...) at most 2 rows name the same one
- intersection_rows: int32 [4096, 4], replicated, may hold values from 0 to 31
- smoothing: float32 [256, 2048], P('gx', 'gy'), may hold values from 0.04 to 0.24
Outputs:
- face_field: float32 [32, 256, 2048], P('lev', 'gx', 'gy')
The draws below stay inside these ranges and needn't reach their ends.
Inputs may be any that keep to these rules, and one draw needn't show every extreme that they name: `intersection_devices`: each row names 4 different source tiles. Among the rows of one destination device (32 aligned rows), no source tile is named more than 2 times, and in every draw some source tile is named exactly 2 times.
All inputs are finite; a program needn't handle non-finite values.
Results may differ from the reference program's by a relative error of at most 0.00011.
Values sent between devices are 32-bit elements; how exact they have to be, the bound alone decides.
No kernel may reach another device: no remote copies, remote signals or barrier semaphores. Data moves between devices by JAX's collectives and lax.ppermute only.
A program may use at most 64 MiB of HBM per device.

```python
import math
import jax
import jax.numpy as jnp
import numpy as np
from jax import lax

BLOCK = 128
K = 4
PASSES = 3
SLAT = 32
FX = 32
CAP = 2
LEV = 32
NLAT = 512
NLON = 1024
NX = 256
NY = 2048
NROWS = 4096
N_GX = 8
N_GY = 16


def draw_remap_weights(key, part):
    key_diag = jax.random.fold_in(key, 11)
    key_off = jax.random.fold_in(key, 12)
    gains = jax.random.uniform(key_diag, (NROWS, K, 1, BLOCK), jnp.float32, 0.6, 1.4)
    spread = jax.random.uniform(key_off, (NROWS, K, BLOCK, BLOCK), jnp.float32, 0.0, 2.0)
    diagonal = (jnp.arange(BLOCK)[:, None] == jnp.arange(BLOCK)[None, :]).astype(jnp.float32)
    return 0.5 / K * gains * diagonal + 0.5 / (K * BLOCK) * spread


def place_ends(entries, stream_key, least, largest):
    extent = entries.shape
    index_at = [jax.random.randint(jax.random.fold_in(stream_key, axis), (), 0, extent[axis]) for axis in range(len(extent))]
    entries = entries.at[tuple(index_at)].set(least)
    longest = extent.index(max(extent))
    index_at[longest] = (index_at[longest] + 1) % extent[longest]
    return entries.at[tuple(index_at)].set(largest)


def levels(rng, extent, pieces, least, high):
    def one(dim, shards_of):
        heights = jax.random.uniform(jax.random.fold_in(jax.random.fold_in(rng, 6), dim), (shards_of,), jnp.float32, least / len(pieces), high / len(pieces))
        return jnp.repeat(jnp.exp(heights), extent[dim] // shards_of).reshape((-1,) + (1,) * (len(extent) - dim - 1))

    factor_of = one(*pieces[0])
    for cut in pieces[1:]:
        factor_of = factor_of * one(*cut)
    return factor_of


def routed_block(rng, own, number, rows, count, top, most, slope):
    sequence = jax.random.permutation(rng, count)
    packed, ordinary = load_shares(count, rows * top, most, slope, True), load_shares(count, rows * top, most, slope, False)
    places = jnp.arange(count)

    def named(tallies, turn):
        used = int((tallies > 0).sum())
        fixed = max(1, used // 4)
        moved = fixed + (places - fixed + turn * (used - fixed)) % max(1, count - fixed)
        return jnp.zeros((count,), jnp.int32).at[sequence[jnp.where(places < fixed, places, moved)]].set(jnp.asarray(tallies, jnp.int32))

    tallies = jnp.where(number % 4 == 0, named(packed, number // 4), named(ordinary, number - number // 4 - 1))
    mixed = jax.random.permutation(jax.random.fold_in(own, 3), count)
    source_of, sink = mixed[0:count // 2 * 2:2], mixed[1:count // 2 * 2:2]
    slack = jnp.minimum(tallies[source_of] - 1, most - tallies[sink]) // 2
    slack = jnp.where((source_of == sequence[0]) | (sink == sequence[0]) | (tallies[sink] == 0), 0, jnp.maximum(slack, 0))
    moved = jax.random.randint(jax.random.fold_in(own, 4), (count // 2,), 0, 1 << 20) % (slack + 1)
    tallies = tallies.at[source_of].add(-moved).at[sink].add(moved)
    members = jnp.searchsorted(jnp.cumsum(tallies), jnp.arange(rows * top), side="right").astype(jnp.int32)
    grid = members.reshape(top, rows).T
    grid = grid[jax.random.permutation(jax.random.fold_in(own, 1), rows)]
    turn = jax.random.randint(jax.random.fold_in(own, 2), (rows, 1), 0, top)
    return jnp.take_along_axis(grid, (jnp.arange(top)[None, :] + turn) % top, axis=1)


def load_shares(count, total, reach, lean, full):
    portions = [(1 << 20) // math.isqrt(rank ** lean) + 1 for rank in range(1, count + 1)]
    largest = reach if full else min(reach, max(-(-total // count), total * portions[0] // sum(portions)))
    least = 1 if total - largest >= count - 1 else 0
    given, spare = [largest] + [least] * (count - 1), total - largest - least * (count - 1)
    while spare > 0:
        movable = [i for i in range(1, count) if given[i] < largest] or [i for i in range(1, count) if given[i] < reach]
        pool, remaining = sum([portions[i] for i in movable]), spare
        for i in movable:
            addition = min(reach - given[i], max(1, remaining * portions[i] // pool), spare)
            given[i] = given[i] + addition
            spare = spare - addition
    return np.array(given)


def noise(stream_key, dims, scale, most, pieces=(), dtype=jnp.bfloat16):
    level = levels(stream_key, dims, pieces, -0.22, 0.18) if pieces else 1.0
    drawn = jax.random.normal(stream_key, dims, jnp.float32) * scale * level
    return jnp.minimum(jnp.maximum(drawn, -most), most).astype(dtype)


def setup_inputs(seed: int = 0) -> dict:
    keys = jax.random.split(jax.random.key(seed), 6)
    source = noise(keys[0], (LEV, NLAT, NLON), 1.0, 6.0, ((0, 2), (1, 16), (2, 8)), jnp.float32)
    remap_weights = draw_remap_weights(jax.random.fold_in(keys[5], 71), 0)
    intersection_devices_keys = jax.random.split(jax.random.fold_in(keys[2], 1), NROWS // FX)
    intersection_devices_turns = jax.random.permutation(jax.random.fold_in(keys[2], 3), NROWS // FX)
    intersection_devices = jax.vmap(lambda own, number: routed_block(jax.random.fold_in(keys[2], 2), own, number, FX, N_GX * N_GY, K, CAP, 1))(intersection_devices_keys, intersection_devices_turns).reshape((NROWS, K))
    intersection_rows = place_ends(jax.random.randint(keys[3], (NROWS, K), 0, SLAT), jax.random.fold_in(keys[3], 1), 0, SLAT - 1).astype(jnp.int32)
    smoothing = jnp.clip(0.04 + 0.19999999552965164 * jax.random.uniform(keys[4], (NX, NY), jnp.float32) ** levels(keys[4], (NX, NY), ((0, 8), (1, 16)), -0.2, 0.2), 0.04, 0.24)
    return {"source": source, "remap_weights": remap_weights, "intersection_devices": intersection_devices, "intersection_rows": intersection_rows, "smoothing": smoothing}


def reference(source, remap_weights, intersection_devices, intersection_rows, smoothing):
    devices = N_GX * N_GY
    grouped = source.reshape(LEV, N_GY, SLAT, N_GX, BLOCK)
    lon_tile = (intersection_devices // N_GY).reshape(devices, FX, K)
    lat_tile = (intersection_devices % N_GY).reshape(devices, FX, K)
    lat_rows = intersection_rows.reshape(devices, FX, K)
    weights = remap_weights.reshape(devices, FX, K, BLOCK, BLOCK)

    def per_device(item):
        lon_part, lat_part, row_part, weight_part = item
        blocks = grouped[:, lat_part, row_part, lon_part, :]
        return jnp.einsum("likc,ikcd->lid", blocks, weight_part, precision=lax.Precision.HIGHEST)

    result = lax.map(per_device, (lon_tile, lat_tile, lat_rows, weights))
    field = result.reshape(N_GX, N_GY, LEV, FX, BLOCK).transpose(2, 0, 3, 1, 4).reshape(LEV, NX, NY)
    for _ in range(PASSES):
        padded = jnp.pad(field, ((0, 0), (1, 1), (1, 1)))
        laplace = padded[:, 2:, 1:-1] + padded[:, :-2, 1:-1] + padded[:, 1:-1, 2:] + padded[:, 1:-1, :-2] - 4.0 * field
        field = field + smoothing * laplace
    return field
```

```python
import jax
import jax.numpy as jnp
from jax import lax
from jax.sharding import PartitionSpec as P

PASSES = 3
CAP = 2


def with_halo(block, axis, dim, width):
    count = lax.axis_size(axis)
    forward = [(i, i + 1) for i in range(count - 1)]
    backward = [(target, source) for source, target in forward]
    low = lax.ppermute(
        lax.slice_in_dim(block, block.shape[dim] - width, None, axis=dim), axis, forward
    )
    high = lax.ppermute(lax.slice_in_dim(block, 0, width, axis=dim), axis, backward)
    return jnp.concatenate([low, block, high], axis=dim)


def smooth_step(values, gained):
    laplace = (
        values[:, 2:, 1:-1]
        + values[:, :-2, 1:-1]
        + values[:, 1:-1, 2:]
        + values[:, 1:-1, :-2]
        - 4.0 * values[:, 1:-1, 1:-1]
    )
    return values[:, 1:-1, 1:-1] + gained * laplace


def shards(source, remap_weights, intersection_devices, intersection_rows, smoothing):
    along_x = lax.axis_size("gx")
    along_y = lax.axis_size("gy")
    devices = along_x * along_y
    frows, fanin, block = remap_weights.shape[:3]
    levels = source.shape[0]
    myself = lax.axis_index("gx") * along_y + lax.axis_index("gy")

    entries = intersection_devices.reshape(devices, frows * fanin)
    lat_all = intersection_rows.reshape(devices, frows * fanin)
    hits = (entries == myself).astype(jnp.int32)
    slot = jnp.cumsum(hits, axis=1) - hits
    slot_ids = jnp.arange(CAP, dtype=jnp.int32)
    chosen = jnp.logical_and(hits[:, None, :] > 0, slot[:, None, :] == slot_ids[None, :, None])
    send_row = jnp.sum(jnp.where(chosen, lat_all[:, None, :], 0), axis=2).reshape(devices * CAP)
    rows_first = jnp.transpose(source, (1, 0, 2))
    outgoing = jnp.take(rows_first, send_row, axis=0)
    incoming = lax.all_to_all(outgoing, ("gx", "gy"), 0, 0, tiled=True)

    mine = lax.dynamic_index_in_dim(entries, myself, 0, keepdims=False)
    order = jnp.arange(frows * fanin)
    earlier = jnp.logical_and(mine[:, None] == mine[None, :], order[None, :] < order[:, None])
    mine_slot = jnp.sum(earlier.astype(jnp.int32), axis=1)
    picked = jnp.take(incoming, mine * CAP + mine_slot, axis=0)
    picked = picked.reshape(frows, fanin, levels, block)
    field = jnp.einsum(
        "iklc,ikcd->lid", picked, remap_weights, precision=lax.Precision.HIGHEST
    )

    carried = jnp.concatenate([field, smoothing[None]], axis=0)
    carried = with_halo(carried, "gx", 1, PASSES)
    carried = with_halo(carried, "gy", 2, PASSES)
    field, gain = carried[:levels], carried[levels:]
    for _ in range(PASSES):
        gain = gain[:, 1:-1, 1:-1]
        field = smooth_step(field, gain)
    return field


def solution(mesh):
    return jax.shard_map(
        shards,
        mesh=mesh,
        in_specs=(P("lev", "gy", "gx"), P(("gx", "gy"), None, None, None), P(), P(), P("gx", "gy")),
        out_specs=P("lev", "gx", "gy"),
        check_vma=False,
    )
```

```python
import jax
import jax.numpy as jnp
from jax import lax
from jax.sharding import PartitionSpec as P

PASSES = 3
CAP = 2


def with_halo(block, axis, dim, width):
    count = lax.axis_size(axis)
    forward = [(i, i + 1) for i in range(count - 1)]
    backward = [(target, source) for source, target in forward]
    low = lax.ppermute(
        lax.slice_in_dim(block, block.shape[dim] - width, None, axis=dim), axis, forward
    )
    high = lax.ppermute(lax.slice_in_dim(block, 0, width, axis=dim), axis, backward)
    return jnp.concatenate([low, block, high], axis=dim)


def packed_halo(block, axis, width):
    count = lax.axis_size(axis)
    forward = [(i, i + 1) for i in range(count - 1)]
    backward = [(target, source) for source, target in forward]
    channels, rows, cols = block.shape
    size = channels * rows * width
    padded = -(-size // 1024) * 1024

    def pack(part):
        flat = jnp.transpose(part, (2, 0, 1)).reshape(size)
        return jnp.pad(flat, (0, padded - size)).reshape(padded // 128, 128)

    def unpack(tile):
        flat = tile.reshape(padded)[:size]
        return jnp.transpose(flat.reshape(width, channels, rows), (1, 2, 0))

    low = unpack(lax.ppermute(pack(block[:, :, cols - width:]), axis, forward))
    high = unpack(lax.ppermute(pack(block[:, :, :width]), axis, backward))
    return jnp.concatenate([low, block, high], axis=2)


def smooth_step(values, gained):
    laplace = (
        values[:, 2:, 1:-1]
        + values[:, :-2, 1:-1]
        + values[:, 1:-1, 2:]
        + values[:, 1:-1, :-2]
        - 4.0 * values[:, 1:-1, 1:-1]
    )
    return values[:, 1:-1, 1:-1] + gained * laplace


def shards(source, remap_weights, intersection_devices, intersection_rows, smoothing):
    along_x = lax.axis_size("gx")
    along_y = lax.axis_size("gy")
    devices = along_x * along_y
    frows, fanin, block = remap_weights.shape[:3]
    levels = source.shape[0]
    myself = lax.axis_index("gx") * along_y + lax.axis_index("gy")

    entries = intersection_devices.reshape(devices, frows * fanin)
    lat_all = intersection_rows.reshape(devices, frows * fanin)
    hits = (entries == myself).astype(jnp.int32)
    slot = jnp.cumsum(hits, axis=1) - hits
    slot_ids = jnp.arange(CAP, dtype=jnp.int32)
    chosen = jnp.logical_and(hits[:, None, :] > 0, slot[:, None, :] == slot_ids[None, :, None])
    send_row = jnp.sum(jnp.where(chosen, lat_all[:, None, :], 0), axis=2).reshape(devices * CAP)
    rows_first = jnp.transpose(source, (1, 0, 2))
    outgoing = jnp.take(rows_first, send_row, axis=0)
    incoming = lax.all_to_all(outgoing, ("gx", "gy"), 0, 0, tiled=True)

    mine = lax.dynamic_index_in_dim(entries, myself, 0, keepdims=False)
    order = jnp.arange(frows * fanin)
    earlier = jnp.logical_and(mine[:, None] == mine[None, :], order[None, :] < order[:, None])
    mine_slot = jnp.sum(earlier.astype(jnp.int32), axis=1)
    picked = jnp.take(incoming, mine * CAP + mine_slot, axis=0)
    picked = picked.reshape(frows, fanin, levels, block)
    field = jnp.einsum(
        "iklc,ikcd->lid", picked, remap_weights, precision=lax.Precision.HIGHEST
    )

    carried = jnp.concatenate([field, smoothing[None]], axis=0)
    carried = with_halo(carried, "gx", 1, PASSES)
    carried = packed_halo(carried, "gy", PASSES)
    field, gain = carried[:levels], carried[levels:]
    for _ in range(PASSES):
        gain = gain[:, 1:-1, 1:-1]
        field = smooth_step(field, gain)
    return field


def solution(mesh):
    return jax.shard_map(
        shards,
        mesh=mesh,
        in_specs=(P("lev", "gy", "gx"), P(("gx", "gy"), None, None, None), P(), P(), P("gx", "gy")),
        out_specs=P("lev", "gx", "gy"),
        check_vma=False,
    )
```

```python
import jax
import jax.numpy as jnp
from jax import lax
from jax.sharding import PartitionSpec as P

PASSES = 3
CAP = 2


def with_halo(block, axis, dim, width):
    count = lax.axis_size(axis)
    forward = [(i, i + 1) for i in range(count - 1)]
    backward = [(target, source) for source, target in forward]
    low = lax.ppermute(
        lax.slice_in_dim(block, block.shape[dim] - width, None, axis=dim), axis, forward
    )
    high = lax.ppermute(lax.slice_in_dim(block, 0, width, axis=dim), axis, backward)
    return jnp.concatenate([low, block, high], axis=dim)


def packed_halo(block, axis, width):
    count = lax.axis_size(axis)
    forward = [(i, i + 1) for i in range(count - 1)]
    backward = [(target, source) for source, target in forward]
    channels, rows, cols = block.shape
    size = channels * rows * width
    padded = -(-size // 1024) * 1024

    def pack(part):
        flat = jnp.transpose(part, (2, 0, 1)).reshape(size)
        return jnp.pad(flat, (0, padded - size)).reshape(padded // 128, 128)

    def unpack(tile):
        flat = tile.reshape(padded)[:size]
        return jnp.transpose(flat.reshape(width, channels, rows), (1, 2, 0))

    low = unpack(lax.ppermute(pack(block[:, :, cols - width:]), axis, forward))
    high = unpack(lax.ppermute(pack(block[:, :, :width]), axis, backward))
    return jnp.concatenate([low, block, high], axis=2)


def smooth_step(values, gained):
    laplace = (
        values[:, 2:, 1:-1]
        + values[:, :-2, 1:-1]
        + values[:, 1:-1, 2:]
        + values[:, 1:-1, :-2]
        - 4.0 * values[:, 1:-1, 1:-1]
    )
    return values[:, 1:-1, 1:-1] + gained * laplace


def shards(source, remap_weights, intersection_devices, intersection_rows, smoothing):
    along_x = lax.axis_size("gx")
    along_y = lax.axis_size("gy")
    devices = along_x * along_y
    frows, fanin, block = remap_weights.shape[:3]
    levels = source.shape[0]
    myself = lax.axis_index("gx") * along_y + lax.axis_index("gy")

    ids_t = intersection_devices.T
    rows_t = intersection_rows.T
    hit_k = ids_t == myself
    hit = jnp.any(hit_k, axis=0).astype(jnp.int32).reshape(devices, frows)
    lat = jnp.sum(jnp.where(hit_k, rows_t, 0), axis=0).reshape(devices, frows)
    slot = jnp.cumsum(hit, axis=1) - hit
    slot_ids = jnp.arange(CAP, dtype=jnp.int32)
    chosen = jnp.logical_and(hit[:, None, :] > 0, slot[:, None, :] == slot_ids[None, :, None])
    send_row = jnp.sum(jnp.where(chosen, lat[:, None, :], 0), axis=2).reshape(devices * CAP)
    rows_first = jnp.transpose(source, (1, 0, 2))
    outgoing = jnp.take(rows_first, send_row, axis=0, mode="clip")
    incoming = lax.all_to_all(outgoing, ("gx", "gy"), 0, 0, tiled=True)

    mine = lax.dynamic_slice_in_dim(ids_t, myself * frows, frows, axis=1).T.reshape(frows * fanin)
    order = jnp.arange(frows * fanin)
    earlier = jnp.logical_and(mine[:, None] == mine[None, :], order[None, :] < order[:, None])
    mine_slot = jnp.sum(earlier.astype(jnp.int32), axis=1)
    picked = jnp.take(incoming, mine * CAP + mine_slot, axis=0, mode="clip")
    picked = picked.reshape(frows, fanin, levels, block)
    field = jnp.einsum(
        "iklc,ikcd->lid", picked, remap_weights, precision=lax.Precision.HIGH
    )

    carried = jnp.concatenate([field, smoothing[None]], axis=0)
    carried = with_halo(carried, "gx", 1, PASSES)
    carried = packed_halo(carried, "gy", PASSES)
    field, gain = carried[:levels], carried[levels:]
    for _ in range(PASSES):
        gain = gain[:, 1:-1, 1:-1]
        field = smooth_step(field, gain)
    return field


def solution(mesh):
    return jax.shard_map(
        shards,
        mesh=mesh,
        in_specs=(P("lev", "gy", "gx"), P(("gx", "gy"), None, None, None), P(), P(), P("gx", "gy")),
        out_specs=P("lev", "gx", "gy"),
        check_vma=False,
    )
```

```python
import jax
import jax.numpy as jnp
from jax import lax
from jax.sharding import PartitionSpec as P

PASSES = 3
CAP = 2


def with_halo(block, axis, dim, width):
    count = lax.axis_size(axis)
    forward = [(i, i + 1) for i in range(count - 1)]
    backward = [(target, source) for source, target in forward]
    low = lax.ppermute(
        lax.slice_in_dim(block, block.shape[dim] - width, None, axis=dim), axis, forward
    )
    high = lax.ppermute(lax.slice_in_dim(block, 0, width, axis=dim), axis, backward)
    return jnp.concatenate([low, block, high], axis=dim)


def packed_halo(block, axis, width):
    count = lax.axis_size(axis)
    forward = [(i, i + 1) for i in range(count - 1)]
    backward = [(target, source) for source, target in forward]
    channels, rows, cols = block.shape
    size = channels * rows * width
    padded = -(-size // 1024) * 1024

    def pack(part):
        flat = jnp.transpose(part, (2, 0, 1)).reshape(size)
        return jnp.pad(flat, (0, padded - size)).reshape(padded // 128, 128)

    def unpack(tile):
        flat = tile.reshape(padded)[:size]
        return jnp.transpose(flat.reshape(width, channels, rows), (1, 2, 0))

    low = unpack(lax.ppermute(pack(block[:, :, cols - width:]), axis, forward))
    high = unpack(lax.ppermute(pack(block[:, :, :width]), axis, backward))
    return jnp.concatenate([low, block, high], axis=2)


def smooth_step(values, gained):
    laplace = (
        values[:, 2:, 1:-1]
        + values[:, :-2, 1:-1]
        + values[:, 1:-1, 2:]
        + values[:, 1:-1, :-2]
        - 4.0 * values[:, 1:-1, 1:-1]
    )
    return values[:, 1:-1, 1:-1] + gained * laplace


def shards(source, remap_weights, intersection_devices, intersection_rows, smoothing):
    along_x = lax.axis_size("gx")
    along_y = lax.axis_size("gy")
    devices = along_x * along_y
    frows, fanin, block = remap_weights.shape[:3]
    levels = source.shape[0]
    myself = lax.axis_index("gx") * along_y + lax.axis_index("gy")

    ids_t = intersection_devices.T
    rows_t = intersection_rows.T
    hit_k = ids_t == myself
    hit = jnp.any(hit_k, axis=0).astype(jnp.int32).reshape(devices, frows)
    lat = jnp.sum(jnp.where(hit_k, rows_t, 0), axis=0).reshape(devices, frows)
    slot = jnp.cumsum(hit, axis=1) - hit
    slot_ids = jnp.arange(CAP, dtype=jnp.int32)
    chosen = jnp.logical_and(hit[:, None, :] > 0, slot[:, None, :] == slot_ids[None, :, None])
    send_row = jnp.sum(jnp.where(chosen, lat[:, None, :], 0), axis=2).reshape(devices * CAP)
    rows_first = jnp.transpose(source, (1, 0, 2))
    outgoing = jnp.take(rows_first, send_row, axis=0, mode="clip")
    incoming = lax.all_to_all(outgoing, ("gx", "gy"), 0, 0, tiled=True)

    mine = lax.dynamic_slice_in_dim(ids_t, myself * frows, frows, axis=1).T.reshape(frows * fanin)
    order = jnp.arange(frows * fanin)
    earlier = jnp.logical_and(mine[:, None] == mine[None, :], order[None, :] < order[:, None])
    mine_slot = jnp.sum(earlier.astype(jnp.int32), axis=1)
    picked = jnp.take(incoming, mine * CAP + mine_slot, axis=0, mode="clip")
    picked = picked.reshape(frows, fanin, levels, block)

    def remap(lo, hi):
        return jnp.einsum(
            "iklc,ikcd->lid", picked[lo:hi], remap_weights[lo:hi], precision=lax.Precision.HIGH
        )

    count = lax.axis_size("gx")
    forward = [(i, i + 1) for i in range(count - 1)]
    backward = [(target, source) for source, target in forward]
    top = jnp.concatenate([remap(0, PASSES), smoothing[None, :PASSES]], axis=0)
    bottom = jnp.concatenate(
        [remap(frows - PASSES, frows), smoothing[None, frows - PASSES:]], axis=0
    )
    top, bottom = lax.optimization_barrier((top, bottom))
    low = lax.ppermute(bottom, "gx", forward)
    high = lax.ppermute(top, "gx", backward)
    middle = jnp.concatenate(
        [remap(PASSES, frows - PASSES), smoothing[None, PASSES:frows - PASSES]], axis=0
    )
    carried = jnp.concatenate([low, top, middle, bottom, high], axis=1)
    carried = packed_halo(carried, "gy", PASSES)
    field, gain = carried[:levels], carried[levels:]
    for _ in range(PASSES):
        gain = gain[:, 1:-1, 1:-1]
        field = smooth_step(field, gain)
    return field


def solution(mesh):
    return jax.shard_map(
        shards,
        mesh=mesh,
        in_specs=(P("lev", "gy", "gx"), P(("gx", "gy"), None, None, None), P(), P(), P("gx", "gy")),
        out_specs=P("lev", "gx", "gy"),
        check_vma=False,
    )
```

```python
import jax
import jax.numpy as jnp
from jax import lax
from jax.sharding import PartitionSpec as P

PASSES = 3
CAP = 2


def chain(count, step):
    return [(i, i + step) for i in range(count) if 0 <= i + step < count]


def pack(part):
    size = part.size
    padded = -(-size // 1024) * 1024
    flat = jnp.transpose(part, (2, 0, 1)).reshape(size)
    return jnp.pad(flat, (0, padded - size)).reshape(padded // 128, 128)


def unpack(tile, shape):
    channels, rows, cols = shape
    flat = tile.reshape(tile.size)[: channels * rows * cols]
    return jnp.transpose(flat.reshape(cols, channels, rows), (1, 2, 0))


def with_halo(block, width):
    nx, ny = lax.axis_size("gx"), lax.axis_size("gy")
    channels, rows, cols = block.shape
    w = width
    low_r = lax.ppermute(block[:, rows - w:], "gx", chain(nx, 1))
    high_r = lax.ppermute(block[:, :w], "gx", chain(nx, -1))
    side = (channels, rows, w)
    low_c = unpack(lax.ppermute(pack(block[:, :, cols - w:]), "gy", chain(ny, 1)), side)
    high_c = unpack(lax.ppermute(pack(block[:, :, :w]), "gy", chain(ny, -1)), side)

    def corner(dx, dy):
        part = block[:, rows - w:] if dx > 0 else block[:, :w]
        part = part[:, :, cols - w:] if dy > 0 else part[:, :, :w]
        pairs = [
            (a * ny + b, (a + dx) * ny + b + dy)
            for a in range(nx)
            for b in range(ny)
            if 0 <= a + dx < nx and 0 <= b + dy < ny
        ]
        return unpack(lax.ppermute(pack(part), ("gx", "gy"), pairs), (channels, w, w))

    upper = jnp.concatenate([corner(1, 1), low_r, corner(1, -1)], axis=2)
    centre = jnp.concatenate([low_c, block, high_c], axis=2)
    lower = jnp.concatenate([corner(-1, 1), high_r, corner(-1, -1)], axis=2)
    return jnp.concatenate([upper, centre, lower], axis=1)


def smooth_step(values, gained):
    laplace = (
        values[:, 2:, 1:-1]
        + values[:, :-2, 1:-1]
        + values[:, 1:-1, 2:]
        + values[:, 1:-1, :-2]
        - 4.0 * values[:, 1:-1, 1:-1]
    )
    return values[:, 1:-1, 1:-1] + gained * laplace


def shards(source, remap_weights, intersection_devices, intersection_rows, smoothing):
    along_x = lax.axis_size("gx")
    along_y = lax.axis_size("gy")
    devices = along_x * along_y
    frows, fanin, block = remap_weights.shape[:3]
    levels = source.shape[0]
    myself = lax.axis_index("gx") * along_y + lax.axis_index("gy")

    ids_t = intersection_devices.T
    rows_t = intersection_rows.T
    hit_k = ids_t == myself
    hit = jnp.any(hit_k, axis=0).astype(jnp.int32).reshape(devices, frows)
    lat = jnp.sum(jnp.where(hit_k, rows_t, 0), axis=0).reshape(devices, frows)
    slot = jnp.cumsum(hit, axis=1) - hit
    slot_ids = jnp.arange(CAP, dtype=jnp.int32)
    chosen = jnp.logical_and(hit[:, None, :] > 0, slot[:, None, :] == slot_ids[None, :, None])
    send_row = jnp.sum(jnp.where(chosen, lat[:, None, :], 0), axis=2).reshape(devices * CAP)
    rows_first = jnp.transpose(source, (1, 0, 2))
    outgoing = jnp.take(rows_first, send_row, axis=0, mode="clip")
    incoming = lax.all_to_all(outgoing, ("gx", "gy"), 0, 0, tiled=True)

    mine = lax.dynamic_slice_in_dim(ids_t, myself * frows, frows, axis=1).T.reshape(frows * fanin)
    order = jnp.arange(frows * fanin)
    earlier = jnp.logical_and(mine[:, None] == mine[None, :], order[None, :] < order[:, None])
    mine_slot = jnp.sum(earlier.astype(jnp.int32), axis=1)
    picked = jnp.take(incoming, mine * CAP + mine_slot, axis=0, mode="clip")
    picked = picked.reshape(frows, fanin, levels, block)

    field = jnp.einsum(
        "iklc,ikcd->lid", picked, remap_weights, precision=lax.Precision.HIGH
    )

    carried = with_halo(jnp.concatenate([field, smoothing[None]], axis=0), PASSES)
    field, gain = carried[:levels], carried[levels:]
    for _ in range(PASSES):
        gain = gain[:, 1:-1, 1:-1]
        field = smooth_step(field, gain)
    return field


def solution(mesh):
    return jax.shard_map(
        shards,
        mesh=mesh,
        in_specs=(P("lev", "gy", "gx"), P(("gx", "gy"), None, None, None), P(), P(), P("gx", "gy")),
        out_specs=P("lev", "gx", "gy"),
        check_vma=False,
    )
```

```python
import jax
import jax.numpy as jnp
from jax import lax
from jax.sharding import PartitionSpec as P

PASSES = 3
CAP = 2


def with_halo(block, axis, dim, width):
    count = lax.axis_size(axis)
    forward = [(i, i + 1) for i in range(count - 1)]
    backward = [(target, source) for source, target in forward]
    low = lax.ppermute(
        lax.slice_in_dim(block, block.shape[dim] - width, None, axis=dim), axis, forward
    )
    high = lax.ppermute(lax.slice_in_dim(block, 0, width, axis=dim), axis, backward)
    return jnp.concatenate([low, block, high], axis=dim)


def packed_halo(block, axis, width):
    count = lax.axis_size(axis)
    forward = [(i, i + 1) for i in range(count - 1)]
    backward = [(target, source) for source, target in forward]
    channels, rows, cols = block.shape
    size = channels * rows * width
    padded = -(-size // 1024) * 1024

    def pack(part):
        flat = jnp.transpose(part, (2, 0, 1)).reshape(size)
        return jnp.pad(flat, (0, padded - size)).reshape(padded // 128, 128)

    def unpack(tile):
        flat = tile.reshape(padded)[:size]
        return jnp.transpose(flat.reshape(width, channels, rows), (1, 2, 0))

    low = unpack(lax.ppermute(pack(block[:, :, cols - width:]), axis, forward))
    high = unpack(lax.ppermute(pack(block[:, :, :width]), axis, backward))
    return jnp.concatenate([low, block, high], axis=2)


def smooth_step(values, gained):
    laplace = (
        values[:, 2:, 1:-1]
        + values[:, :-2, 1:-1]
        + values[:, 1:-1, 2:]
        + values[:, 1:-1, :-2]
        - 4.0 * values[:, 1:-1, 1:-1]
    )
    return values[:, 1:-1, 1:-1] + gained * laplace


def shards(source, remap_weights, intersection_devices, intersection_rows, smoothing):
    along_x = lax.axis_size("gx")
    along_y = lax.axis_size("gy")
    devices = along_x * along_y
    frows, fanin, block = remap_weights.shape[:3]
    levels = source.shape[0]
    myself = lax.axis_index("gx") * along_y + lax.axis_index("gy")

    ids_t = intersection_devices.T
    rows_t = intersection_rows.T
    hit_k = ids_t == myself
    hit = jnp.any(hit_k, axis=0).astype(jnp.int32).reshape(devices, frows)
    lat = jnp.sum(jnp.where(hit_k, rows_t, 0), axis=0).reshape(devices, frows)
    slot = jnp.cumsum(hit, axis=1) - hit
    slot_ids = jnp.arange(CAP, dtype=jnp.int32)
    chosen = jnp.logical_and(hit[:, None, :] > 0, slot[:, None, :] == slot_ids[None, :, None])
    send_row = jnp.sum(jnp.where(chosen, lat[:, None, :], 0), axis=2).reshape(devices * CAP)
    onehot = (send_row[:, None] == jnp.arange(source.shape[1])[None, :]).astype(source.dtype)
    outgoing = jnp.einsum("jr,lrc->jlc", onehot, source, precision=lax.Precision.HIGHEST)
    incoming = lax.all_to_all(outgoing, ("gx", "gy"), 0, 0, tiled=True)

    mine = lax.dynamic_slice_in_dim(ids_t, myself * frows, frows, axis=1).T.reshape(frows * fanin)
    order = jnp.arange(frows * fanin)
    earlier = jnp.logical_and(mine[:, None] == mine[None, :], order[None, :] < order[:, None])
    mine_slot = jnp.sum(earlier.astype(jnp.int32), axis=1)
    picked = jnp.take(incoming, mine * CAP + mine_slot, axis=0, mode="clip")
    picked = picked.reshape(frows, fanin, levels, block)

    def remap(lo, hi):
        return jnp.einsum(
            "iklc,ikcd->lid", picked[lo:hi], remap_weights[lo:hi], precision=lax.Precision.HIGH
        )

    count = lax.axis_size("gx")
    forward = [(i, i + 1) for i in range(count - 1)]
    backward = [(target, source) for source, target in forward]
    top = jnp.concatenate([remap(0, PASSES), smoothing[None, :PASSES]], axis=0)
    bottom = jnp.concatenate(
        [remap(frows - PASSES, frows), smoothing[None, frows - PASSES:]], axis=0
    )
    top, bottom = lax.optimization_barrier((top, bottom))
    low = lax.ppermute(bottom, "gx", forward)
    high = lax.ppermute(top, "gx", backward)
    middle = jnp.concatenate(
        [remap(PASSES, frows - PASSES), smoothing[None, PASSES:frows - PASSES]], axis=0
    )
    carried = jnp.concatenate([low, top, middle, bottom, high], axis=1)
    carried = packed_halo(carried, "gy", PASSES)
    field, gain = carried[:levels], carried[levels:]
    for _ in range(PASSES):
        gain = gain[:, 1:-1, 1:-1]
        field = smooth_step(field, gain)
    return field


def solution(mesh):
    return jax.shard_map(
        shards,
        mesh=mesh,
        in_specs=(P("lev", "gy", "gx"), P(("gx", "gy"), None, None, None), P(), P(), P("gx", "gy")),
        out_specs=P("lev", "gx", "gy"),
        check_vma=False,
    )
```

```python
import jax
import jax.numpy as jnp
from jax import lax
from jax.sharding import PartitionSpec as P

PASSES = 3
CAP = 2


def with_halo(block, axis, dim, width):
    count = lax.axis_size(axis)
    forward = [(i, i + 1) for i in range(count - 1)]
    backward = [(target, source) for source, target in forward]
    low = lax.ppermute(
        lax.slice_in_dim(block, block.shape[dim] - width, None, axis=dim), axis, forward
    )
    high = lax.ppermute(lax.slice_in_dim(block, 0, width, axis=dim), axis, backward)
    return jnp.concatenate([low, block, high], axis=dim)


def packed_halo(block, axis, width):
    count = lax.axis_size(axis)
    forward = [(i, i + 1) for i in range(count - 1)]
    backward = [(target, source) for source, target in forward]
    channels, rows, cols = block.shape
    size = channels * rows * width
    padded = -(-size // 1024) * 1024

    def pack(part):
        flat = jnp.transpose(part, (2, 0, 1)).reshape(size)
        return jnp.pad(flat, (0, padded - size)).reshape(padded // 128, 128)

    def unpack(tile):
        flat = tile.reshape(padded)[:size]
        return jnp.transpose(flat.reshape(width, channels, rows), (1, 2, 0))

    low = unpack(lax.ppermute(pack(block[:, :, cols - width:]), axis, forward))
    high = unpack(lax.ppermute(pack(block[:, :, :width]), axis, backward))
    return jnp.concatenate([low, block, high], axis=2)


def smooth_step(values, gained):
    laplace = (
        values[:, 2:, 1:-1]
        + values[:, :-2, 1:-1]
        + values[:, 1:-1, 2:]
        + values[:, 1:-1, :-2]
        - 4.0 * values[:, 1:-1, 1:-1]
    )
    return values[:, 1:-1, 1:-1] + gained * laplace


def shards(source, remap_weights, intersection_devices, intersection_rows, smoothing):
    along_x = lax.axis_size("gx")
    along_y = lax.axis_size("gy")
    devices = along_x * along_y
    frows, fanin, block = remap_weights.shape[:3]
    levels = source.shape[0]
    myself = lax.axis_index("gx") * along_y + lax.axis_index("gy")

    ids_t = intersection_devices.T
    rows_t = intersection_rows.T
    code = jnp.sum(jnp.where(ids_t == myself, rows_t + 1, 0), axis=0).reshape(devices, frows)
    hit = (code > 0).astype(jnp.int32)
    lat = code - 1
    slot = jnp.cumsum(hit, axis=1) - hit
    slot_ids = jnp.arange(CAP, dtype=jnp.int32)
    chosen = jnp.logical_and(hit[:, None, :] > 0, slot[:, None, :] == slot_ids[None, :, None])
    send_row = jnp.sum(jnp.where(chosen, lat[:, None, :], 0), axis=2).reshape(devices * CAP)
    rows_first = jnp.transpose(source, (1, 0, 2))
    outgoing = jnp.take(rows_first, send_row, axis=0, mode="clip")
    incoming = lax.all_to_all(outgoing, ("gx", "gy"), 0, 0, tiled=True)

    mine = lax.dynamic_slice_in_dim(ids_t, myself * frows, frows, axis=1).T.reshape(frows * fanin)
    order = jnp.arange(frows * fanin)
    earlier = jnp.logical_and(mine[:, None] == mine[None, :], order[None, :] < order[:, None])
    mine_slot = jnp.sum(earlier.astype(jnp.int32), axis=1)
    picked = jnp.take(incoming, mine * CAP + mine_slot, axis=0, mode="clip")
    picked = picked.reshape(frows, fanin, levels, block)

    def remap(lo, hi):
        return jnp.einsum(
            "iklc,ikcd->lid", picked[lo:hi], remap_weights[lo:hi], precision=lax.Precision.HIGH
        )

    count = lax.axis_size("gx")
    forward = [(i, i + 1) for i in range(count - 1)]
    backward = [(target, source) for source, target in forward]
    top = jnp.concatenate([remap(0, PASSES), smoothing[None, :PASSES]], axis=0)
    bottom = jnp.concatenate(
        [remap(frows - PASSES, frows), smoothing[None, frows - PASSES:]], axis=0
    )
    top, bottom = lax.optimization_barrier((top, bottom))
    low = lax.ppermute(bottom, "gx", forward)
    high = lax.ppermute(top, "gx", backward)
    middle = jnp.concatenate(
        [remap(PASSES, frows - PASSES), smoothing[None, PASSES:frows - PASSES]], axis=0
    )
    carried = jnp.concatenate([low, top, middle, bottom, high], axis=1)
    carried = packed_halo(carried, "gy", PASSES)
    field, gain = carried[:levels], carried[levels:]
    for _ in range(PASSES):
        gain = gain[:, 1:-1, 1:-1]
        field = smooth_step(field, gain)
    return field


def solution(mesh):
    return jax.shard_map(
        shards,
        mesh=mesh,
        in_specs=(P("lev", "gy", "gx"), P(("gx", "gy"), None, None, None), P(), P(), P("gx", "gy")),
        out_specs=P("lev", "gx", "gy"),
        check_vma=False,
    )
```

```python
import jax
import jax.numpy as jnp
from jax import lax
from jax.sharding import PartitionSpec as P

PASSES = 3
CAP = 2


def with_halo(block, axis, dim, width):
    count = lax.axis_size(axis)
    forward = [(i, i + 1) for i in range(count - 1)]
    backward = [(target, source) for source, target in forward]
    low = lax.ppermute(
        lax.slice_in_dim(block, block.shape[dim] - width, None, axis=dim), axis, forward
    )
    high = lax.ppermute(lax.slice_in_dim(block, 0, width, axis=dim), axis, backward)
    return jnp.concatenate([low, block, high], axis=dim)


def packed_halo(block, axis, width):
    count = lax.axis_size(axis)
    forward = [(i, i + 1) for i in range(count - 1)]
    backward = [(target, source) for source, target in forward]
    channels, rows, cols = block.shape
    size = channels * rows * width
    padded = -(-size // 1024) * 1024

    def pack(part):
        flat = jnp.transpose(part, (2, 0, 1)).reshape(size)
        return jnp.pad(flat, (0, padded - size)).reshape(padded // 128, 128)

    def unpack(tile):
        flat = tile.reshape(padded)[:size]
        return jnp.transpose(flat.reshape(width, channels, rows), (1, 2, 0))

    low = unpack(lax.ppermute(pack(block[:, :, cols - width:]), axis, forward))
    high = unpack(lax.ppermute(pack(block[:, :, :width]), axis, backward))
    return jnp.concatenate([low, block, high], axis=2)


def smooth_step(values, gained):
    laplace = (
        values[:, 2:, 1:-1]
        + values[:, :-2, 1:-1]
        + values[:, 1:-1, 2:]
        + values[:, 1:-1, :-2]
        - 4.0 * values[:, 1:-1, 1:-1]
    )
    return values[:, 1:-1, 1:-1] + gained * laplace


def shards(source, remap_weights, intersection_devices, intersection_rows, smoothing):
    along_x = lax.axis_size("gx")
    along_y = lax.axis_size("gy")
    devices = along_x * along_y
    frows, fanin, block = remap_weights.shape[:3]
    levels = source.shape[0]
    myself = lax.axis_index("gx") * along_y + lax.axis_index("gy")

    ids_t = intersection_devices.T
    rows_t = intersection_rows.T
    code = jnp.sum(jnp.where(ids_t == myself, rows_t + 1, 0), axis=0).reshape(devices, frows)
    hit = (code > 0).astype(jnp.int32)
    lat = code - 1
    slot = jnp.cumsum(hit, axis=1) - hit
    slot_ids = jnp.arange(CAP, dtype=jnp.int32)
    chosen = jnp.logical_and(hit[:, None, :] > 0, slot[:, None, :] == slot_ids[None, :, None])
    send_row = jnp.sum(jnp.where(chosen, lat[:, None, :], 0), axis=2).reshape(devices * CAP)
    rows_first = jnp.transpose(source, (1, 0, 2))
    outgoing = jnp.take(rows_first, send_row, axis=0, mode="clip")
    incoming = lax.all_to_all(outgoing, ("gx", "gy"), 0, 0, tiled=True)

    mine = lax.dynamic_slice_in_dim(ids_t, myself * frows, frows, axis=1).T.reshape(frows * fanin)
    order = jnp.arange(frows * fanin)
    earlier = jnp.logical_and(mine[:, None] == mine[None, :], order[None, :] < order[:, None])
    mine_slot = jnp.sum(earlier.astype(jnp.int32), axis=1)
    picked = jnp.take(incoming, mine * CAP + mine_slot, axis=0, mode="clip")
    picked = picked.reshape(frows, fanin, levels, block)

    def remap(lo, hi):
        return jnp.einsum(
            "iklc,ikcd->lid", picked[lo:hi], remap_weights[lo:hi], precision=lax.Precision.HIGH
        )

    count = lax.axis_size("gx")
    forward = [(i, i + 1) for i in range(count - 1)]
    backward = [(target, source) for source, target in forward]
    edge_rows = lambda a: jnp.concatenate([a[:PASSES], a[frows - PASSES:]], axis=0)
    edges = jnp.einsum(
        "iklc,ikcd->lid",
        edge_rows(picked),
        edge_rows(remap_weights),
        precision=lax.Precision.HIGH,
    )
    top = jnp.concatenate([edges[:, :PASSES], smoothing[None, :PASSES]], axis=0)
    bottom = jnp.concatenate([edges[:, PASSES:], smoothing[None, frows - PASSES:]], axis=0)
    top, bottom = lax.optimization_barrier((top, bottom))
    low = lax.ppermute(bottom, "gx", forward)
    high = lax.ppermute(top, "gx", backward)
    middle = jnp.concatenate(
        [remap(PASSES, frows - PASSES), smoothing[None, PASSES:frows - PASSES]], axis=0
    )
    carried = jnp.concatenate([low, top, middle, bottom, high], axis=1)
    carried = packed_halo(carried, "gy", PASSES)
    field, gain = carried[:levels], carried[levels:]
    for _ in range(PASSES):
        gain = gain[:, 1:-1, 1:-1]
        field = smooth_step(field, gain)
    return field


def solution(mesh):
    return jax.shard_map(
        shards,
        mesh=mesh,
        in_specs=(P("lev", "gy", "gx"), P(("gx", "gy"), None, None, None), P(), P(), P("gx", "gy")),
        out_specs=P("lev", "gx", "gy"),
        check_vma=False,
    )
```

```python
import jax
import jax.numpy as jnp
from jax import lax
from jax.sharding import PartitionSpec as P

PASSES = 3
CAP = 2


def with_halo(block, axis, dim, width):
    count = lax.axis_size(axis)
    forward = [(i, i + 1) for i in range(count - 1)]
    backward = [(target, source) for source, target in forward]
    low = lax.ppermute(
        lax.slice_in_dim(block, block.shape[dim] - width, None, axis=dim), axis, forward
    )
    high = lax.ppermute(lax.slice_in_dim(block, 0, width, axis=dim), axis, backward)
    return jnp.concatenate([low, block, high], axis=dim)


def packed_halo(block, axis, width):
    count = lax.axis_size(axis)
    forward = [(i, i + 1) for i in range(count - 1)]
    backward = [(target, source) for source, target in forward]
    channels, rows, cols = block.shape
    size = channels * rows * width
    padded = -(-size // 1024) * 1024

    def pack(part):
        flat = jnp.transpose(part, (2, 0, 1)).reshape(size)
        return jnp.pad(flat, (0, padded - size)).reshape(padded // 128, 128)

    def unpack(tile):
        flat = tile.reshape(padded)[:size]
        return jnp.transpose(flat.reshape(width, channels, rows), (1, 2, 0))

    low = unpack(lax.ppermute(pack(block[:, :, cols - width:]), axis, forward))
    high = unpack(lax.ppermute(pack(block[:, :, :width]), axis, backward))
    return jnp.concatenate([low, block, high], axis=2)


def smooth_step(values, gained):
    laplace = (
        values[:, 2:, 1:-1]
        + values[:, :-2, 1:-1]
        + values[:, 1:-1, 2:]
        + values[:, 1:-1, :-2]
        - 4.0 * values[:, 1:-1, 1:-1]
    )
    return values[:, 1:-1, 1:-1] + gained * laplace


def shards(source, remap_weights, intersection_devices, intersection_rows, smoothing):
    along_x = lax.axis_size("gx")
    along_y = lax.axis_size("gy")
    devices = along_x * along_y
    frows, fanin, block = remap_weights.shape[:3]
    levels = source.shape[0]
    myself = lax.axis_index("gx") * along_y + lax.axis_index("gy")

    ids_t = intersection_devices.T
    rows_t = intersection_rows.T
    code = jnp.sum(jnp.where(ids_t == myself, rows_t + 1, 0), axis=0).reshape(devices, frows)
    hit = (code > 0).astype(jnp.int32)
    lat = code - 1
    slot = jnp.cumsum(hit, axis=1) - hit
    slot_ids = jnp.arange(CAP, dtype=jnp.int32)
    chosen = jnp.logical_and(hit[:, None, :] > 0, slot[:, None, :] == slot_ids[None, :, None])
    send_row = jnp.sum(jnp.where(chosen, lat[:, None, :], 0), axis=2).reshape(devices * CAP)
    rows_first = jnp.transpose(source, (1, 0, 2))
    outgoing = jnp.take(rows_first, send_row, axis=0, mode="clip")
    incoming = lax.all_to_all(outgoing, ("gx", "gy"), 0, 0, tiled=True)

    mine = lax.dynamic_slice_in_dim(ids_t, myself * frows, frows, axis=1).T.reshape(frows * fanin)
    order = jnp.arange(frows * fanin)
    earlier = jnp.logical_and(mine[:, None] == mine[None, :], order[None, :] < order[:, None])
    mine_slot = jnp.sum(earlier.astype(jnp.int32), axis=1)
    picked = jnp.take(incoming, mine * CAP + mine_slot, axis=0, mode="clip")
    picked = picked.reshape(frows, fanin, levels, block)

    def remap(lo, hi):
        return jnp.einsum(
            "iklc,ikcd->lid", picked[lo:hi], remap_weights[lo:hi], precision=lax.Precision.HIGH
        )

    count = lax.axis_size("gx")
    forward = [(i, i + 1) for i in range(count - 1)]
    backward = [(target, source) for source, target in forward]
    gain = packed_halo(with_halo(smoothing[None], "gx", 1, PASSES), "gy", PASSES)
    edge_rows = lambda a: jnp.concatenate([a[:PASSES], a[frows - PASSES:]], axis=0)
    edges = jnp.einsum(
        "iklc,ikcd->lid",
        edge_rows(picked),
        edge_rows(remap_weights),
        precision=lax.Precision.HIGH,
    )
    top, bottom = lax.optimization_barrier((edges[:, :PASSES], edges[:, PASSES:]))
    low = lax.ppermute(bottom, "gx", forward)
    high = lax.ppermute(top, "gx", backward)
    middle = remap(PASSES, frows - PASSES)
    carried = jnp.concatenate([low, top, middle, bottom, high], axis=1)
    field = packed_halo(carried, "gy", PASSES)
    for _ in range(PASSES):
        gain = gain[:, 1:-1, 1:-1]
        field = smooth_step(field, gain)
    return field


def solution(mesh):
    return jax.shard_map(
        shards,
        mesh=mesh,
        in_specs=(P("lev", "gy", "gx"), P(("gx", "gy"), None, None, None), P(), P(), P("gx", "gy")),
        out_specs=P("lev", "gx", "gy"),
        check_vma=False,
    )
```

```python
import jax
import jax.numpy as jnp
from jax import lax
from jax.sharding import PartitionSpec as P

PASSES = 3
CAP = 2


def with_halo(block, axis, dim, width):
    count = lax.axis_size(axis)
    forward = [(i, i + 1) for i in range(count - 1)]
    backward = [(target, source) for source, target in forward]
    low = lax.ppermute(
        lax.slice_in_dim(block, block.shape[dim] - width, None, axis=dim), axis, forward
    )
    high = lax.ppermute(lax.slice_in_dim(block, 0, width, axis=dim), axis, backward)
    return jnp.concatenate([low, block, high], axis=dim)


def packed_strips(block, axis, width):
    count = lax.axis_size(axis)
    forward = [(i, i + 1) for i in range(count - 1)]
    backward = [(target, source) for source, target in forward]
    channels, rows, cols = block.shape
    size = channels * rows * width
    padded = -(-size // 1024) * 1024

    def pack(part):
        flat = jnp.transpose(part, (2, 0, 1)).reshape(size)
        return jnp.pad(flat, (0, padded - size)).reshape(padded // 128, 128)

    def unpack(tile):
        flat = tile.reshape(padded)[:size]
        return jnp.transpose(flat.reshape(width, channels, rows), (1, 2, 0))

    low = unpack(lax.ppermute(pack(block[:, :, cols - width:]), axis, forward))
    high = unpack(lax.ppermute(pack(block[:, :, :width]), axis, backward))
    return low, high


def packed_halo(block, axis, width):
    low, high = packed_strips(block, axis, width)
    return jnp.concatenate([low, block, high], axis=2)


def smooth_step(values, gained):
    laplace = (
        values[:, 2:, 1:-1]
        + values[:, :-2, 1:-1]
        + values[:, 1:-1, 2:]
        + values[:, 1:-1, :-2]
        - 4.0 * values[:, 1:-1, 1:-1]
    )
    return values[:, 1:-1, 1:-1] + gained * laplace


def shards(source, remap_weights, intersection_devices, intersection_rows, smoothing):
    along_x = lax.axis_size("gx")
    along_y = lax.axis_size("gy")
    devices = along_x * along_y
    frows, fanin, block = remap_weights.shape[:3]
    levels = source.shape[0]
    myself = lax.axis_index("gx") * along_y + lax.axis_index("gy")

    ids_t = intersection_devices.T
    rows_t = intersection_rows.T
    code = jnp.sum(jnp.where(ids_t == myself, rows_t + 1, 0), axis=0).reshape(devices, frows)
    hit = (code > 0).astype(jnp.int32)
    lat = code - 1
    slot = jnp.cumsum(hit, axis=1) - hit
    slot_ids = jnp.arange(CAP, dtype=jnp.int32)
    chosen = jnp.logical_and(hit[:, None, :] > 0, slot[:, None, :] == slot_ids[None, :, None])
    send_row = jnp.sum(jnp.where(chosen, lat[:, None, :], 0), axis=2).reshape(devices * CAP)
    rows_first = jnp.transpose(source, (1, 0, 2))
    outgoing = jnp.take(rows_first, send_row, axis=0, mode="clip")
    incoming = lax.all_to_all(outgoing, ("gx", "gy"), 0, 0, tiled=True)

    mine = lax.dynamic_slice_in_dim(ids_t, myself * frows, frows, axis=1).T.reshape(frows * fanin)
    order = jnp.arange(frows * fanin)
    earlier = jnp.logical_and(mine[:, None] == mine[None, :], order[None, :] < order[:, None])
    mine_slot = jnp.sum(earlier.astype(jnp.int32), axis=1)
    picked = jnp.take(incoming, mine * CAP + mine_slot, axis=0, mode="clip")
    picked = picked.reshape(frows, fanin, levels, block)

    def remap(lo, hi):
        return jnp.einsum(
            "iklc,ikcd->lid", picked[lo:hi], remap_weights[lo:hi], precision=lax.Precision.HIGH
        )

    count = lax.axis_size("gx")
    forward = [(i, i + 1) for i in range(count - 1)]
    backward = [(target, source) for source, target in forward]
    gain = packed_halo(with_halo(smoothing[None], "gx", 1, PASSES), "gy", PASSES)
    edge_rows = lambda a: jnp.concatenate([a[:PASSES], a[frows - PASSES:]], axis=0)
    edges = jnp.einsum(
        "iklc,ikcd->lid",
        edge_rows(picked),
        edge_rows(remap_weights),
        precision=lax.Precision.HIGH,
    )
    top, bottom = lax.optimization_barrier((edges[:, :PASSES], edges[:, PASSES:]))
    low = lax.ppermute(bottom, "gx", forward)
    high = lax.ppermute(top, "gx", backward)
    middle = remap(PASSES, frows - PASSES)
    carried = jnp.concatenate([low, top, middle, bottom, high], axis=1)
    low_c, high_c = packed_strips(carried, "gy", PASSES)

    def passes(values, gained):
        for step in range(1, PASSES + 1):
            values = smooth_step(values, gained[:, step:gained.shape[1] - step, step:gained.shape[2] - step])
        return values

    cols = carried.shape[2]
    inner = passes(carried, gain[:, :, PASSES:PASSES + cols])
    left = passes(
        jnp.concatenate([low_c, carried[:, :, :2 * PASSES]], axis=2), gain[:, :, :3 * PASSES]
    )
    right = passes(
        jnp.concatenate([carried[:, :, cols - 2 * PASSES:], high_c], axis=2),
        gain[:, :, cols - PASSES:],
    )
    return jnp.concatenate([left, inner, right], axis=2)


def solution(mesh):
    return jax.shard_map(
        shards,
        mesh=mesh,
        in_specs=(P("lev", "gy", "gx"), P(("gx", "gy"), None, None, None), P(), P(), P("gx", "gy")),
        out_specs=P("lev", "gx", "gy"),
        check_vma=False,
    )
```

```python
import jax
import jax.numpy as jnp
from jax import lax
from jax.sharding import PartitionSpec as P

PASSES = 3
CAP = 2


def with_halo(block, axis, dim, width):
    count = lax.axis_size(axis)
    forward = [(i, i + 1) for i in range(count - 1)]
    backward = [(target, source) for source, target in forward]
    low = lax.ppermute(
        lax.slice_in_dim(block, block.shape[dim] - width, None, axis=dim), axis, forward
    )
    high = lax.ppermute(lax.slice_in_dim(block, 0, width, axis=dim), axis, backward)
    return jnp.concatenate([low, block, high], axis=dim)


def packed_halo(block, axis, width):
    count = lax.axis_size(axis)
    forward = [(i, i + 1) for i in range(count - 1)]
    backward = [(target, source) for source, target in forward]
    channels, rows, cols = block.shape
    size = channels * rows * width
    padded = -(-size // 1024) * 1024

    def pack(part):
        flat = jnp.transpose(part, (2, 0, 1)).reshape(size)
        return jnp.pad(flat, (0, padded - size)).reshape(padded // 128, 128)

    def unpack(tile):
        flat = tile.reshape(padded)[:size]
        return jnp.transpose(flat.reshape(width, channels, rows), (1, 2, 0))

    low = unpack(lax.ppermute(pack(block[:, :, cols - width:]), axis, forward))
    high = unpack(lax.ppermute(pack(block[:, :, :width]), axis, backward))
    return jnp.concatenate([low, block, high], axis=2)


def smooth_step(values, gained):
    laplace = (
        values[:, 2:, 1:-1]
        + values[:, :-2, 1:-1]
        + values[:, 1:-1, 2:]
        + values[:, 1:-1, :-2]
        - 4.0 * values[:, 1:-1, 1:-1]
    )
    return values[:, 1:-1, 1:-1] + gained * laplace


def shards(source, remap_weights, intersection_devices, intersection_rows, smoothing):
    along_x = lax.axis_size("gx")
    along_y = lax.axis_size("gy")
    devices = along_x * along_y
    frows, fanin, block = remap_weights.shape[:3]
    levels = source.shape[0]
    myself = lax.axis_index("gx") * along_y + lax.axis_index("gy")

    ids_t = intersection_devices.T
    rows_t = intersection_rows.T
    code = jnp.sum(jnp.where(ids_t == myself, rows_t + 1, 0), axis=0).reshape(devices, frows)
    hit = (code > 0).astype(jnp.int32)
    lat = code - 1
    slot = jnp.cumsum(hit, axis=1) - hit
    slot_ids = jnp.arange(CAP, dtype=jnp.int32)
    chosen = jnp.logical_and(hit[:, None, :] > 0, slot[:, None, :] == slot_ids[None, :, None])
    send_row = jnp.sum(jnp.where(chosen, lat[:, None, :], 0), axis=2).reshape(devices * CAP)
    rows_first = jnp.transpose(source, (1, 0, 2))
    outgoing = jnp.take(rows_first, send_row, axis=0, mode="clip")
    incoming = lax.all_to_all(outgoing, ("gx", "gy"), 0, 0, tiled=True)

    mine = lax.dynamic_slice_in_dim(ids_t, myself * frows, frows, axis=1).T.reshape(frows * fanin)
    order = jnp.arange(frows * fanin)
    earlier = jnp.logical_and(mine[:, None] == mine[None, :], order[None, :] < order[:, None])
    mine_slot = jnp.sum(earlier.astype(jnp.int32), axis=1)
    picked = jnp.take(incoming, mine * CAP + mine_slot, axis=0, mode="clip")
    picked = picked.reshape(frows, fanin, levels, block)

    def remap(lo, hi):
        return jnp.einsum(
            "iklc,ikcd->lid", picked[lo:hi], remap_weights[lo:hi], precision=lax.Precision.HIGH
        )

    count = lax.axis_size("gx")
    forward = [(i, i + 1) for i in range(count - 1)]
    backward = [(target, source) for source, target in forward]
    gain = packed_halo(with_halo(smoothing[None], "gx", 1, PASSES), "gy", PASSES)
    edge_rows = lambda a: jnp.concatenate([a[:PASSES], a[frows - PASSES:]], axis=0)
    edges = jnp.einsum(
        "iklc,ikcd->lid",
        edge_rows(picked),
        edge_rows(remap_weights),
        precision=lax.Precision.HIGH,
    )
    top, bottom = lax.optimization_barrier((edges[:, :PASSES], edges[:, PASSES:]))
    low = lax.ppermute(bottom, "gx", forward)
    top, middle = lax.optimization_barrier((top, remap(PASSES, frows - PASSES)))
    high = lax.ppermute(top, "gx", backward)
    carried = jnp.concatenate([low, top, middle, bottom, high], axis=1)
    field = packed_halo(carried, "gy", PASSES)
    for _ in range(PASSES):
        gain = gain[:, 1:-1, 1:-1]
        field = smooth_step(field, gain)
    return field


def solution(mesh):
    return jax.shard_map(
        shards,
        mesh=mesh,
        in_specs=(P("lev", "gy", "gx"), P(("gx", "gy"), None, None, None), P(), P(), P("gx", "gy")),
        out_specs=P("lev", "gx", "gy"),
        check_vma=False,
    )
```

```python
import jax
import jax.numpy as jnp
from jax import lax
from jax.sharding import PartitionSpec as P

PASSES = 3
CAP = 2


def with_halo(block, axis, dim, width):
    count = lax.axis_size(axis)
    forward = [(i, i + 1) for i in range(count - 1)]
    backward = [(target, source) for source, target in forward]
    low = lax.ppermute(
        lax.slice_in_dim(block, block.shape[dim] - width, None, axis=dim), axis, forward
    )
    high = lax.ppermute(lax.slice_in_dim(block, 0, width, axis=dim), axis, backward)
    return jnp.concatenate([low, block, high], axis=dim)


def packed_halo(block, axis, width):
    count = lax.axis_size(axis)
    forward = [(i, i + 1) for i in range(count - 1)]
    backward = [(target, source) for source, target in forward]
    channels, rows, cols = block.shape
    size = channels * rows * width
    padded = -(-size // 1024) * 1024

    def pack(part):
        flat = jnp.transpose(part, (2, 0, 1)).reshape(size)
        return jnp.pad(flat, (0, padded - size)).reshape(padded // 128, 128)

    def unpack(tile):
        flat = tile.reshape(padded)[:size]
        return jnp.transpose(flat.reshape(width, channels, rows), (1, 2, 0))

    low = unpack(lax.ppermute(pack(block[:, :, cols - width:]), axis, forward))
    high = unpack(lax.ppermute(pack(block[:, :, :width]), axis, backward))
    return jnp.concatenate([low, block, high], axis=2)


def smooth_step(values, gained):
    laplace = (
        values[:, 2:, 1:-1]
        + values[:, :-2, 1:-1]
        + values[:, 1:-1, 2:]
        + values[:, 1:-1, :-2]
        - 4.0 * values[:, 1:-1, 1:-1]
    )
    return values[:, 1:-1, 1:-1] + gained * laplace


def shards(source, remap_weights, intersection_devices, intersection_rows, smoothing):
    along_x = lax.axis_size("gx")
    along_y = lax.axis_size("gy")
    devices = along_x * along_y
    frows, fanin, block = remap_weights.shape[:3]
    levels = source.shape[0]
    myself = lax.axis_index("gx") * along_y + lax.axis_index("gy")

    ids_t = intersection_devices.T
    rows_t = intersection_rows.T
    code = jnp.sum(jnp.where(ids_t == myself, rows_t + 1, 0), axis=0).reshape(devices, frows)
    hit = (code > 0).astype(jnp.int32)
    lat = code - 1
    slot = jnp.cumsum(hit, axis=1) - hit
    slot_ids = jnp.arange(CAP, dtype=jnp.int32)
    chosen = jnp.logical_and(hit[:, None, :] > 0, slot[:, None, :] == slot_ids[None, :, None])
    send_row = jnp.sum(jnp.where(chosen, lat[:, None, :], 0), axis=2).reshape(devices * CAP)
    rows_first = jnp.transpose(source, (1, 0, 2))
    outgoing = jnp.take(rows_first, send_row, axis=0, mode="clip")
    incoming = lax.all_to_all(outgoing, ("gx", "gy"), 0, 0, tiled=True)

    mine = lax.dynamic_slice_in_dim(ids_t, myself * frows, frows, axis=1).T.reshape(frows * fanin)
    order = jnp.arange(frows * fanin)
    earlier = jnp.logical_and(mine[:, None] == mine[None, :], order[None, :] < order[:, None])
    mine_slot = jnp.sum(earlier.astype(jnp.int32), axis=1)
    picked = jnp.take(incoming, mine * CAP + mine_slot, axis=0, mode="clip")
    picked = picked.reshape(frows, fanin, levels, block)

    def split(x):
        high = lax.reduce_precision(x, exponent_bits=8, mantissa_bits=7)
        return high.astype(jnp.bfloat16), (x - high).astype(jnp.bfloat16)

    w_hi, w_lo = split(remap_weights)
    p_hi, p_lo = split(picked)

    def product(a, w):
        return jnp.einsum("iklc,ikcd->lid", a, w, preferred_element_type=jnp.float32)

    def remap_parts(pick):
        both = product(jnp.concatenate([pick(p_hi), pick(p_lo)], axis=2), pick(w_hi))
        return (both[:levels] + both[levels:]) + product(pick(p_hi), pick(w_lo))

    def remap(lo, hi):
        return remap_parts(lambda a: a[lo:hi])

    count = lax.axis_size("gx")
    forward = [(i, i + 1) for i in range(count - 1)]
    backward = [(target, source) for source, target in forward]
    gain = packed_halo(with_halo(smoothing[None], "gx", 1, PASSES), "gy", PASSES)
    edge_rows = lambda a: jnp.concatenate([a[:PASSES], a[frows - PASSES:]], axis=0)
    edges = remap_parts(edge_rows)
    top, bottom = lax.optimization_barrier((edges[:, :PASSES], edges[:, PASSES:]))
    low = lax.ppermute(bottom, "gx", forward)
    high = lax.ppermute(top, "gx", backward)
    middle = remap(PASSES, frows - PASSES)
    carried = jnp.concatenate([low, top, middle, bottom, high], axis=1)
    field = packed_halo(carried, "gy", PASSES)
    for _ in range(PASSES):
        gain = gain[:, 1:-1, 1:-1]
        field = smooth_step(field, gain)
    return field


def solution(mesh):
    return jax.shard_map(
        shards,
        mesh=mesh,
        in_specs=(P("lev", "gy", "gx"), P(("gx", "gy"), None, None, None), P(), P(), P("gx", "gy")),
        out_specs=P("lev", "gx", "gy"),
        check_vma=False,
    )
```

```python
import jax
import jax.numpy as jnp
from jax import lax
from jax.sharding import PartitionSpec as P

PASSES = 3
CAP = 2


def with_halo(block, axis, dim, width):
    count = lax.axis_size(axis)
    forward = [(i, i + 1) for i in range(count - 1)]
    backward = [(target, source) for source, target in forward]
    low = lax.ppermute(
        lax.slice_in_dim(block, block.shape[dim] - width, None, axis=dim), axis, forward
    )
    high = lax.ppermute(lax.slice_in_dim(block, 0, width, axis=dim), axis, backward)
    return jnp.concatenate([low, block, high], axis=dim)


def packed_halo(block, axis, width):
    count = lax.axis_size(axis)
    forward = [(i, i + 1) for i in range(count - 1)]
    backward = [(target, source) for source, target in forward]
    channels, rows, cols = block.shape
    size = channels * rows * width
    padded = -(-size // 1024) * 1024

    def pack(part):
        flat = jnp.transpose(part, (1, 0, 2)).reshape(size)
        return jnp.pad(flat, (0, padded - size)).reshape(padded // 128, 128)

    def unpack(tile):
        flat = tile.reshape(padded)[:size]
        return jnp.transpose(flat.reshape(rows, channels, width), (1, 0, 2))

    low = unpack(lax.ppermute(pack(block[:, :, cols - width:]), axis, forward))
    high = unpack(lax.ppermute(pack(block[:, :, :width]), axis, backward))
    return jnp.concatenate([low, block, high], axis=2)


def smooth_step(values, gained):
    laplace = (
        values[:, 2:, 1:-1]
        + values[:, :-2, 1:-1]
        + values[:, 1:-1, 2:]
        + values[:, 1:-1, :-2]
        - 4.0 * values[:, 1:-1, 1:-1]
    )
    return values[:, 1:-1, 1:-1] + gained * laplace


def shards(source, remap_weights, intersection_devices, intersection_rows, smoothing):
    along_x = lax.axis_size("gx")
    along_y = lax.axis_size("gy")
    devices = along_x * along_y
    frows, fanin, block = remap_weights.shape[:3]
    levels = source.shape[0]
    myself = lax.axis_index("gx") * along_y + lax.axis_index("gy")

    ids_t = intersection_devices.T
    rows_t = intersection_rows.T
    code = jnp.sum(jnp.where(ids_t == myself, rows_t + 1, 0), axis=0).reshape(devices, frows)
    hit = (code > 0).astype(jnp.int32)
    lat = code - 1
    slot = jnp.cumsum(hit, axis=1) - hit
    slot_ids = jnp.arange(CAP, dtype=jnp.int32)
    chosen = jnp.logical_and(hit[:, None, :] > 0, slot[:, None, :] == slot_ids[None, :, None])
    send_row = jnp.sum(jnp.where(chosen, lat[:, None, :], 0), axis=2).reshape(devices * CAP)
    rows_first = jnp.transpose(source, (1, 0, 2))
    outgoing = jnp.take(rows_first, send_row, axis=0, mode="clip")
    incoming = lax.all_to_all(outgoing, ("gx", "gy"), 0, 0, tiled=True)

    mine = lax.dynamic_slice_in_dim(ids_t, myself * frows, frows, axis=1).T.reshape(frows * fanin)
    order = jnp.arange(frows * fanin)
    earlier = jnp.logical_and(mine[:, None] == mine[None, :], order[None, :] < order[:, None])
    mine_slot = jnp.sum(earlier.astype(jnp.int32), axis=1)
    picked = jnp.take(incoming, mine * CAP + mine_slot, axis=0, mode="clip")
    picked = picked.reshape(frows, fanin, levels, block)

    def split(x):
        high = lax.reduce_precision(x, exponent_bits=8, mantissa_bits=7)
        return high.astype(jnp.bfloat16), (x - high).astype(jnp.bfloat16)

    w_hi, w_lo = split(remap_weights)
    p_hi, p_lo = split(picked)

    def product(a, w):
        return jnp.einsum("iklc,ikcd->lid", a, w, preferred_element_type=jnp.float32)

    def remap_parts(pick):
        both = product(jnp.concatenate([pick(p_hi), pick(p_lo)], axis=2), pick(w_hi))
        return (both[:levels] + both[levels:]) + product(pick(p_hi), pick(w_lo))

    def remap(lo, hi):
        return remap_parts(lambda a: a[lo:hi])

    count = lax.axis_size("gx")
    forward = [(i, i + 1) for i in range(count - 1)]
    backward = [(target, source) for source, target in forward]
    gain = packed_halo(with_halo(smoothing[None], "gx", 1, PASSES), "gy", PASSES)
    edge_rows = lambda a: jnp.concatenate([a[:PASSES], a[frows - PASSES:]], axis=0)
    edges = remap_parts(edge_rows)
    top, bottom = lax.optimization_barrier((edges[:, :PASSES], edges[:, PASSES:]))
    low = lax.ppermute(bottom, "gx", forward)
    high = lax.ppermute(top, "gx", backward)
    middle = remap(PASSES, frows - PASSES)
    carried = jnp.concatenate([low, top, middle, bottom, high], axis=1)
    field = packed_halo(carried, "gy", PASSES)
    for _ in range(PASSES):
        gain = gain[:, 1:-1, 1:-1]
        field = smooth_step(field, gain)
    return field


def solution(mesh):
    return jax.shard_map(
        shards,
        mesh=mesh,
        in_specs=(P("lev", "gy", "gx"), P(("gx", "gy"), None, None, None), P(), P(), P("gx", "gy")),
        out_specs=P("lev", "gx", "gy"),
        check_vma=False,
    )
```

```python
import jax
import jax.numpy as jnp
from jax import lax
from jax.experimental.layout import Layout, with_layout_constraint
from jax.sharding import PartitionSpec as P

PASSES = 3
CAP = 2


def with_halo(block, axis, dim, width):
    count = lax.axis_size(axis)
    forward = [(i, i + 1) for i in range(count - 1)]
    backward = [(target, source) for source, target in forward]
    low = lax.ppermute(
        lax.slice_in_dim(block, block.shape[dim] - width, None, axis=dim), axis, forward
    )
    high = lax.ppermute(lax.slice_in_dim(block, 0, width, axis=dim), axis, backward)
    return jnp.concatenate([low, block, high], axis=dim)


def packed_halo(block, axis, width):
    count = lax.axis_size(axis)
    forward = [(i, i + 1) for i in range(count - 1)]
    backward = [(target, source) for source, target in forward]
    channels, rows, cols = block.shape
    size = channels * rows * width
    padded = -(-size // 1024) * 1024

    def pack(part):
        flat = jnp.transpose(part, (2, 0, 1)).reshape(size)
        return jnp.pad(flat, (0, padded - size)).reshape(padded // 128, 128)

    def unpack(tile):
        flat = tile.reshape(padded)[:size]
        return jnp.transpose(flat.reshape(width, channels, rows), (1, 2, 0))

    low = unpack(lax.ppermute(pack(block[:, :, cols - width:]), axis, forward))
    high = unpack(lax.ppermute(pack(block[:, :, :width]), axis, backward))
    return jnp.concatenate([low, block, high], axis=2)


def smooth_step(values, gained):
    laplace = (
        values[:, 2:, 1:-1]
        + values[:, :-2, 1:-1]
        + values[:, 1:-1, 2:]
        + values[:, 1:-1, :-2]
        - 4.0 * values[:, 1:-1, 1:-1]
    )
    return values[:, 1:-1, 1:-1] + gained * laplace


def shards(source, remap_weights, intersection_devices, intersection_rows, smoothing):
    along_x = lax.axis_size("gx")
    along_y = lax.axis_size("gy")
    devices = along_x * along_y
    frows, fanin, block = remap_weights.shape[:3]
    levels = source.shape[0]
    myself = lax.axis_index("gx") * along_y + lax.axis_index("gy")

    ids_t = intersection_devices.T
    rows_t = intersection_rows.T
    code = jnp.sum(jnp.where(ids_t == myself, rows_t + 1, 0), axis=0).reshape(devices, frows)
    hit = (code > 0).astype(jnp.int32)
    lat = code - 1
    slot = jnp.cumsum(hit, axis=1) - hit
    slot_ids = jnp.arange(CAP, dtype=jnp.int32)
    chosen = jnp.logical_and(hit[:, None, :] > 0, slot[:, None, :] == slot_ids[None, :, None])
    send_row = jnp.sum(jnp.where(chosen, lat[:, None, :], 0), axis=2).reshape(devices * CAP)
    rows_first = jnp.transpose(source, (1, 0, 2))
    outgoing = jnp.take(rows_first, send_row, axis=0, mode="clip")
    incoming = lax.all_to_all(outgoing, ("gx", "gy"), 0, 0, tiled=True)

    mine = lax.dynamic_slice_in_dim(ids_t, myself * frows, frows, axis=1).T.reshape(frows * fanin)
    order = jnp.arange(frows * fanin)
    earlier = jnp.logical_and(mine[:, None] == mine[None, :], order[None, :] < order[:, None])
    mine_slot = jnp.sum(earlier.astype(jnp.int32), axis=1)
    picked = jnp.take(incoming, mine * CAP + mine_slot, axis=0, mode="clip")
    picked = picked.reshape(frows, fanin, levels, block)

    def split(x):
        high = lax.reduce_precision(x, exponent_bits=8, mantissa_bits=7)
        return high.astype(jnp.bfloat16), (x - high).astype(jnp.bfloat16)

    w_hi, w_lo = split(remap_weights)
    p_hi, p_lo = split(picked)

    def product(a, w):
        return jnp.einsum("iklc,ikcd->lid", a, w, preferred_element_type=jnp.float32)

    def remap_parts(pick):
        both = product(jnp.concatenate([pick(p_hi), pick(p_lo)], axis=2), pick(w_hi))
        return (both[:levels] + both[levels:]) + product(pick(p_hi), pick(w_lo))

    def remap(lo, hi):
        return remap_parts(lambda a: a[lo:hi])

    count = lax.axis_size("gx")
    forward = [(i, i + 1) for i in range(count - 1)]
    backward = [(target, source) for source, target in forward]
    gain = packed_halo(with_halo(smoothing[None], "gx", 1, PASSES), "gy", PASSES)
    edge_rows = lambda a: jnp.concatenate([a[:PASSES], a[frows - PASSES:]], axis=0)
    edges = remap_parts(edge_rows)
    top, bottom = lax.optimization_barrier((edges[:, :PASSES], edges[:, PASSES:]))
    low = lax.ppermute(bottom, "gx", forward)
    high = lax.ppermute(top, "gx", backward)
    middle = remap(PASSES, frows - PASSES)
    carried = jnp.concatenate([low, top, middle, bottom, high], axis=1)
    field = with_layout_constraint(packed_halo(carried, "gy", PASSES), Layout((0, 1, 2)))
    for _ in range(PASSES):
        gain = gain[:, 1:-1, 1:-1]
        field = smooth_step(field, gain)
    return field


def solution(mesh):
    return jax.shard_map(
        shards,
        mesh=mesh,
        in_specs=(P("lev", "gy", "gx"), P(("gx", "gy"), None, None, None), P(), P(), P("gx", "gy")),
        out_specs=P("lev", "gx", "gy"),
        check_vma=False,
    )
```
